32 devices in a mesh: parts: 2 (over x), chan: 16 (over z, y, core).
Axes of the slice: x: 2, y: 2, z: 4, core: 2. Of those that a mesh axis runs over, the one named last changes fastest.
Arguments:
- spectra: bfloat16 [1024, 8, 1024], P(('parts', 'chan')), parts along dimension 0, may hold values from -8 to 8
- source_blocks: int32 [4, 2], P('parts'), parts along dimension 0, may hold values from 0 to 15
- window_valid: int32 [16], P('parts'), parts along dimension 0, may hold values 0 or 1
Outputs:
- correlations: bfloat16 [2, 2, 32, 1024, 512], P(None, None, None, ('parts', 'chan')), parts along dimension 3
The draws below stay inside these ranges and needn't reach their ends.
There are 2 independent parts, one for each index of `parts`. The reference program is written for one: setup_inputs(seed, part) draws one part's arguments, and reference() takes and returns one part's arrays. A program takes and returns all parts, laid end to end along the dimension named above; each array names one. Nothing has to cross between parts.
All inputs are finite; a program needn't handle non-finite values. Where the reference program divides by a largest or mean magnitude, that divisor is 1e-20 or more.
Results may differ from the reference program's by a relative error of at most 0.0045.
Values may be sent and summed in bfloat16 or wider, within the bound.
No kernel may reach another device: no remote copies, remote signals or barrier semaphores. Data moves between devices by JAX's collectives and lax.ppermute only.
A program may use at most 192 MiB of HBM per device.

```python
import math
import jax
import jax.numpy as jnp
from jax import lax

SOURCE = 32
F = 512
LAGS = 512
STEPS = 2
CH_DEV = 32
W = 8
C = 512
NBLK = 16


def draw_spectra(key, part):
    key_noise = jax.random.fold_in(key, 11)
    key_shared = jax.random.fold_in(key, 12)
    key_sign = jax.random.fold_in(key, 13)
    key_level = jax.random.fold_in(key, 14)
    key_factor = jax.random.fold_in(key, 15)
    noise = jax.random.normal(key_noise, (C, W, 2 * F), jnp.float32)
    low_level = 0.25
    high_level = 2.5
    low_factor = 0.8
    high_factor = 1.25
    shared = jax.random.normal(key_shared, (1, W, 2 * F), jnp.float32)
    signs = jnp.where(jax.random.bernoulli(key_sign, 0.5, (C, 1, 1)), 1.0, -1.0).astype(jnp.float32)
    log_level = jax.random.uniform(key_level, (NBLK, 1, 1, 1), jnp.float32, math.log(low_level), math.log(high_level))
    factor = jax.random.uniform(key_factor, (NBLK, SOURCE, 1, 1), jnp.float32, low_factor, high_factor)
    amplitude = (jnp.exp(log_level) * factor).reshape(C, 1, 1)
    values = amplitude * 0.7 * (noise + signs * shared)
    return jnp.clip(values, -8.0, 8.0).astype(jnp.bfloat16)


def with_ends(array, stream_key, least, top_value):
    shape = array.shape
    spot = [jax.random.randint(jax.random.fold_in(stream_key, axis), (), 0, shape[axis]) for axis in range(len(shape))]
    array = array.at[tuple(spot)].set(least)
    longest = shape.index(max(shape))
    spot[longest] = (spot[longest] + 1) % shape[longest]
    return array.at[tuple(spot)].set(top_value)


def setup_inputs(seed: int = 0, part: int = 0) -> dict:
    arg_keys = jax.random.split(jax.random.key(seed), 4)
    own_keys = jax.random.split(jax.random.fold_in(arg_keys[3], part), 4)
    return {
        "spectra": draw_spectra(jax.random.fold_in(jax.random.fold_in(arg_keys[3], part), 71), part),
        "source_blocks": with_ends(jax.random.randint(own_keys[1], (STEPS, 2), 0, NBLK), jax.random.fold_in(own_keys[1], 1), 0, NBLK - 1).astype(jnp.int32),
        "window_valid": with_ends((jax.random.randint(own_keys[2], (W,), 0, 4) < 3).astype(jnp.int32), jax.random.fold_in(own_keys[2], 1), 0, 1),
    }


def build_table(bins, lags):
    freq = jnp.arange(bins, dtype=jnp.int32)[:, None]
    shifted = jnp.arange(lags, dtype=jnp.int32)[None, :] - lags // 2
    phase = jnp.remainder(freq * shifted, 2 * bins).astype(jnp.float32)
    theta = phase * (2.0 * math.pi / (2 * bins))
    weight = jnp.where(freq == 0, 1.0, 2.0).astype(jnp.float32) / (2 * bins)
    return jnp.concatenate([weight * jnp.cos(theta), -weight * jnp.sin(theta)], axis=0).astype(jnp.bfloat16)


def reference(spectra, source_blocks, window_valid):
    lag_table = build_table(F, LAGS)
    window_mask = window_valid.astype(jnp.bfloat16)[None, :, None]
    receiver_groups = spectra.reshape(C // CH_DEV, CH_DEV, W, 2 * F)
    results = []
    for step in range(STEPS):
        pair = []
        for slot in range(2):
            block_index = source_blocks[step, slot]
            source = lax.dynamic_slice_in_dim(spectra, (block_index * SOURCE).astype(jnp.int32), SOURCE, 0) * window_mask
            real_src = source[..., :F].astype(jnp.float32)
            imag_src = source[..., F:].astype(jnp.float32)

            def one_group(group):
                real_rcv = group[..., :F].astype(jnp.float32)
                imag_rcv = group[..., F:].astype(jnp.float32)
                real_part = jnp.einsum("swf,rwf->srf", real_src, real_rcv) + jnp.einsum("swf,rwf->srf", imag_src, imag_rcv)
                imag_part = jnp.einsum("swf,rwf->srf", real_src, imag_rcv) - jnp.einsum("swf,rwf->srf", imag_src, real_rcv)
                cross = jnp.concatenate([real_part, imag_part], axis=2).astype(jnp.bfloat16)
                flat = cross.reshape(SOURCE * CH_DEV, 2 * F)
                return jnp.dot(flat, lag_table, preferred_element_type=jnp.float32).reshape(SOURCE, CH_DEV, LAGS)

            traces = lax.map(one_group, receiver_groups)
            peak = jnp.max(jnp.abs(traces), axis=(0, 2, 3))
            normed = (traces / (peak[None, :, None, None] + 1e-6)).astype(jnp.bfloat16)
            pair.append(jnp.transpose(normed, (1, 0, 2, 3)).reshape(SOURCE, C, LAGS))
        results.append(jnp.stack(pair, axis=0))
    return jnp.stack(results, axis=0)
```

```python
import math

import jax
import jax.numpy as jnp
from jax import lax
from jax.sharding import PartitionSpec as P

SOURCE = 32
LAGS = 512


def build_table(bins, lags):
    freq = jnp.arange(bins, dtype=jnp.int32)[:, None]
    shifted = jnp.arange(lags, dtype=jnp.int32)[None, :] - lags // 2
    phase = jnp.remainder(freq * shifted, 2 * bins).astype(jnp.float32)
    theta = phase * (2.0 * math.pi / (2 * bins))
    weight = jnp.where(freq == 0, 1.0, 2.0).astype(jnp.float32) / (2 * bins)
    return jnp.concatenate([weight * jnp.cos(theta), -weight * jnp.sin(theta)], axis=0).astype(
        jnp.bfloat16
    )


def plane_size(mesh):
    devs = list(mesh.devices[0])
    n = len(devs)
    best = 1
    for axis in range(3):
        first = next((i for i, d in enumerate(devs) if d.coords[axis] != devs[0].coords[axis]), None)
        if first is not None and first > best:
            best = first
    if best >= n or n % best:
        best = 1
    return best


def pairs_of(n, fn):
    out = []
    for i in range(n):
        j = fn(i)
        if j is not None:
            out.append((i, j))
    return out


def make_shards(n, qc):
    zc = n // qc
    plane_bits = [1 << b for b in reversed(range(qc.bit_length() - 1))]

    def shards(spectra, source_blocks, window_valid):
        receivers, windows, width = spectra.shape
        bins = width // 2
        me = lax.axis_index("chan")
        z = me // qc
        q = me % qc
        blocks = source_blocks.reshape(-1)
        nb = blocks.shape[0]
        zk = blocks // qc
        qk = blocks % qc
        piece = SOURCE // qc

        own = spectra.reshape(qc, piece, windows, width)
        by_off = [lax.dynamic_index_in_dim(own, q, 0, keepdims=False)]
        for d in range(1, qc):
            send = lax.dynamic_index_in_dim(own, q ^ d, 0, keepdims=False)
            by_off.append(
                lax.ppermute(send, "chan", pairs_of(n, lambda i, d=d: (i // qc) * qc + ((i % qc) ^ d)))
            )
        by_off = jnp.stack(by_off)

        here = zk == z
        sel = jnp.take(by_off, qk ^ q, axis=0)
        payload = jnp.where(here[:, None, None, None], sel, jnp.zeros_like(sel))

        up_pairs = pairs_of(n, lambda i: i + qc if i // qc < zc - 1 else None)
        down_pairs = pairs_of(n, lambda i: i - qc if i // qc > 0 else None)
        mask = here[:, None, None, None]
        cur_up, cur_down = payload, payload
        rec_up, rec_down = payload, payload
        for r in range(zc - 1):
            rec_up = lax.ppermute(cur_up, "chan", up_pairs)
            rec_down = lax.ppermute(cur_down, "chan", down_pairs)
            if r < zc - 2:
                cur_up = jnp.where(mask, payload, rec_up)
                cur_down = jnp.where(mask, payload, rec_down)
        below = (z > zk)[:, None, None, None]
        mine = jnp.where(mask, payload, jnp.where(below, rec_up, rec_down))

        offs = [0]
        held = [mine]
        for b in plane_bits:
            got = lax.ppermute(
                jnp.stack(held), "chan", pairs_of(n, lambda i, b=b: (i // qc) * qc + ((i % qc) ^ b))
            )
            offs = offs + [o ^ b for o in offs]
            held = held + [got[i] for i in range(got.shape[0])]
        stack = jnp.stack(held)
        inv = [0] * qc
        for e, o in enumerate(offs):
            inv[o] = e
        inv = jnp.array(inv, jnp.int32)
        order = jnp.take(inv, jnp.arange(qc, dtype=jnp.int32) ^ q)
        full = jnp.take(stack, order, axis=0)
        src_all = jnp.transpose(full, (1, 0, 2, 3, 4)).reshape(nb, SOURCE, windows, width)

        lag_table = build_table(bins, LAGS)
        window_mask = window_valid.astype(jnp.bfloat16)[None, None, :, None]
        src_all = src_all * window_mask
        rr = spectra[..., :bins].astype(jnp.float32)[None, None]
        ri = spectra[..., bins:].astype(jnp.float32)[None, None]
        traces_all = []
        peaks = []
        for k in range(nb):
            src = src_all[k]
            sr = src[..., :bins].astype(jnp.float32)[:, None]
            si = src[..., bins:].astype(jnp.float32)[:, None]
            real_part = jnp.sum(sr * rr[0] + si * ri[0], axis=2)
            imag_part = jnp.sum(sr * ri[0] - si * rr[0], axis=2)
            cross = jnp.concatenate([real_part, imag_part], axis=2).astype(jnp.bfloat16)
            flat = cross.reshape(SOURCE * receivers, width)
            traces = jnp.dot(flat, lag_table, preferred_element_type=jnp.float32).reshape(
                SOURCE, receivers, LAGS
            )
            traces_all.append(traces)
            peaks.append(jnp.max(jnp.abs(traces), axis=(1, 2)))
        peak = jnp.stack(peaks)
        d = 1
        while d < n:
            peak = jnp.maximum(peak, lax.ppermute(peak, "chan", pairs_of(n, lambda i, d=d: i ^ d)))
            d *= 2
        out = [
            (traces_all[k] / (peak[k][:, None, None] + 1e-06)).astype(jnp.bfloat16) for k in range(nb)
        ]
        stacked = jnp.stack(out, axis=0)
        return stacked.reshape(source_blocks.shape[0], source_blocks.shape[1], SOURCE, receivers, LAGS)

    return shards


def solution(mesh):
    n = mesh.shape["chan"]
    qc = plane_size(mesh)
    placed = (P(("parts", "chan"), None, None), P("parts", None), P("parts"))
    return jax.shard_map(
        make_shards(n, qc),
        mesh=mesh,
        in_specs=placed,
        out_specs=P(None, None, None, ("parts", "chan"), None),
        check_vma=False,
    )
```

```python
import math

import jax
import jax.numpy as jnp
from jax import lax
from jax.sharding import PartitionSpec as P

SOURCE = 32
LAGS = 512


def build_table(bins, lags):
    freq = jnp.arange(bins, dtype=jnp.int32)[:, None]
    shifted = jnp.arange(lags, dtype=jnp.int32)[None, :] - lags // 2
    phase = jnp.remainder(freq * shifted, 2 * bins).astype(jnp.float32)
    theta = phase * (2.0 * math.pi / (2 * bins))
    weight = jnp.where(freq == 0, 1.0, 2.0).astype(jnp.float32) / (2 * bins)
    return jnp.concatenate([weight * jnp.cos(theta), -weight * jnp.sin(theta)], axis=0).astype(
        jnp.bfloat16
    )


def plane_size(mesh):
    devs = list(mesh.devices[0])
    n = len(devs)
    best = 1
    for axis in range(3):
        first = next((i for i, d in enumerate(devs) if d.coords[axis] != devs[0].coords[axis]), None)
        if first is not None and first > best:
            best = first
    if best >= n or n % best:
        best = 1
    return best


def pairs_of(n, fn):
    out = []
    for i in range(n):
        j = fn(i)
        if j is not None:
            out.append((i, j))
    return out


def make_shards(n, qc):
    zc = n // qc
    plane_bits = [1 << b for b in reversed(range(qc.bit_length() - 1))]

    def shards(spectra, source_blocks, window_valid):
        receivers, windows, width = spectra.shape
        bins = width // 2
        me = lax.axis_index("chan")
        z = me // qc
        q = me % qc
        blocks = source_blocks.reshape(-1)
        nb = blocks.shape[0]
        zk = blocks // qc
        qk = blocks % qc
        piece = SOURCE // qc

        own = spectra.reshape(qc, piece, windows, width)
        by_off = [lax.dynamic_index_in_dim(own, q, 0, keepdims=False)]
        for d in range(1, qc):
            send = lax.dynamic_index_in_dim(own, q ^ d, 0, keepdims=False)
            by_off.append(
                lax.ppermute(send, "chan", pairs_of(n, lambda i, d=d: (i // qc) * qc + ((i % qc) ^ d)))
            )
        by_off = jnp.stack(by_off)

        up_pairs = pairs_of(n, lambda i: i + qc if i // qc < zc - 1 else None)
        down_pairs = pairs_of(n, lambda i: i - qc if i // qc > 0 else None)
        inv = [0] * qc
        offs = [0]
        for b in plane_bits:
            offs = offs + [o ^ b for o in offs]
        for e, o in enumerate(offs):
            inv[o] = e
        order = jnp.take(jnp.array(inv, jnp.int32), jnp.arange(qc, dtype=jnp.int32) ^ q)

        lag_table = build_table(bins, LAGS)
        window_mask = window_valid.astype(jnp.bfloat16)[None, :, None]
        rr = spectra[..., :bins].astype(jnp.float32)
        ri = spectra[..., bins:].astype(jnp.float32)

        out = []
        for k in range(nb):
            here = zk[k] == z
            sel = lax.dynamic_index_in_dim(by_off, qk[k] ^ q, 0, keepdims=False)
            payload = jnp.where(here, sel, jnp.zeros_like(sel))

            cur_up, cur_down = payload, payload
            rec_up, rec_down = payload, payload
            for r in range(zc - 1):
                rec_up = lax.ppermute(cur_up, "chan", up_pairs)
                rec_down = lax.ppermute(cur_down, "chan", down_pairs)
                if r < zc - 2:
                    cur_up = jnp.where(here, payload, rec_up)
                    cur_down = jnp.where(here, payload, rec_down)
            mine = jnp.where(here, payload, jnp.where(z > zk[k], rec_up, rec_down))

            held = [mine]
            for b in plane_bits:
                got = lax.ppermute(
                    jnp.stack(held), "chan", pairs_of(n, lambda i, b=b: (i // qc) * qc + ((i % qc) ^ b))
                )
                held = held + [got[i] for i in range(got.shape[0])]
            stack = jnp.stack(held)
            full = jnp.take(stack, order, axis=0)
            src = full.reshape(SOURCE, windows, width) * window_mask

            sr = src[..., :bins].astype(jnp.float32)[:, None]
            si = src[..., bins:].astype(jnp.float32)[:, None]
            real_part = jnp.sum(sr * rr + si * ri, axis=2)
            imag_part = jnp.sum(sr * ri - si * rr, axis=2)
            cross = jnp.concatenate([real_part, imag_part], axis=2).astype(jnp.bfloat16)
            flat = cross.reshape(SOURCE * receivers, width)
            traces = jnp.dot(flat, lag_table, preferred_element_type=jnp.float32).reshape(
                SOURCE, receivers, LAGS
            )
            peak = jnp.max(jnp.abs(traces), axis=(1, 2))
            d = 1
            while d < n:
                peak = jnp.maximum(peak, lax.ppermute(peak, "chan", pairs_of(n, lambda i, d=d: i ^ d)))
                d *= 2
            out.append((traces / (peak[:, None, None] + 1e-06)).astype(jnp.bfloat16))
        stacked = jnp.stack(out, axis=0)
        return stacked.reshape(source_blocks.shape[0], source_blocks.shape[1], SOURCE, receivers, LAGS)

    return shards


def solution(mesh):
    n = mesh.shape["chan"]
    qc = plane_size(mesh)
    placed = (P(("parts", "chan"), None, None), P("parts", None), P("parts"))
    return jax.shard_map(
        make_shards(n, qc),
        mesh=mesh,
        in_specs=placed,
        out_specs=P(None, None, None, ("parts", "chan"), None),
        check_vma=False,
    )
```

```python
import math

import jax
import jax.numpy as jnp
from jax import lax
from jax.experimental import pallas as pl
from jax.sharding import PartitionSpec as P

SOURCE = 32
LAGS = 512


def build_table(bins, lags):
    freq = jnp.arange(bins, dtype=jnp.int32)[:, None]
    shifted = jnp.arange(lags, dtype=jnp.int32)[None, :] - lags // 2
    phase = jnp.remainder(freq * shifted, 2 * bins).astype(jnp.float32)
    theta = phase * (2.0 * math.pi / (2 * bins))
    weight = jnp.where(freq == 0, 1.0, 2.0).astype(jnp.float32) / (2 * bins)
    return jnp.concatenate([weight * jnp.cos(theta), -weight * jnp.sin(theta)], axis=0).astype(
        jnp.bfloat16
    )


ST = 8
RC = 16


def cross_kernel(src_ref, rcv_ref, out_ref):
    bins = src_ref.shape[-1] // 2
    windows = src_ref.shape[2]
    rows = rcv_ref.shape[1]

    def body(s, carry):
        row = src_ref[0, s].astype(jnp.float32)
        for c in range(rows // RC):
            rs = slice(c * RC, (c + 1) * RC)
            acc_re = jnp.zeros((RC, bins), jnp.float32)
            acc_im = jnp.zeros((RC, bins), jnp.float32)
            for w in range(windows):
                a = jnp.broadcast_to(row[w : w + 1, :bins], (RC, bins))
                b = jnp.broadcast_to(row[w : w + 1, bins:], (RC, bins))
                rr = rcv_ref[w, rs, :bins]
                ri = rcv_ref[w, rs, bins:]
                acc_re = acc_re + (a * rr + b * ri)
                acc_im = acc_im + (a * ri - b * rr)
            out_ref[0, s, rs, :bins] = acc_re.astype(out_ref.dtype)
            out_ref[0, s, rs, bins:] = acc_im.astype(out_ref.dtype)
        return carry

    lax.fori_loop(0, src_ref.shape[1], body, 0)


def cross_products(src_all, rcv):
    nb, sources, windows, width = src_all.shape
    receivers = rcv.shape[0]
    rcv_t = jnp.transpose(rcv, (1, 0, 2)).astype(jnp.float32)
    flops = 8 * nb * sources * receivers * windows * (width // 2)
    return pl.pallas_call(
        cross_kernel,
        grid=(nb, sources // ST),
        in_specs=[
            pl.BlockSpec((1, ST, windows, width), lambda k, i: (k, i, 0, 0)),
            pl.BlockSpec((windows, receivers, width), lambda k, i: (0, 0, 0)),
        ],
        out_specs=pl.BlockSpec((1, ST, receivers, width), lambda k, i: (k, i, 0, 0)),
        out_shape=jax.ShapeDtypeStruct((nb, sources, receivers, width), jnp.bfloat16),
        cost_estimate=pl.CostEstimate(
            flops=flops,
            bytes_accessed=src_all.size * 2 + rcv_t.size * 4 + nb * sources * receivers * width * 2,
            transcendentals=0,
        ),
    )(src_all, rcv_t)


def plane_size(mesh):
    devs = list(mesh.devices[0])
    n = len(devs)
    best = 1
    for axis in range(3):
        first = next((i for i, d in enumerate(devs) if d.coords[axis] != devs[0].coords[axis]), None)
        if first is not None and first > best:
            best = first
    if best >= n or n % best:
        best = 1
    return best


def pairs_of(n, fn):
    out = []
    for i in range(n):
        j = fn(i)
        if j is not None:
            out.append((i, j))
    return out


def make_shards(n, qc):
    zc = n // qc
    plane_bits = [1 << b for b in reversed(range(qc.bit_length() - 1))]

    def shards(spectra, source_blocks, window_valid):
        receivers, windows, width = spectra.shape
        bins = width // 2
        me = lax.axis_index("chan")
        z = me // qc
        q = me % qc
        blocks = source_blocks.reshape(-1)
        nb = blocks.shape[0]
        zk = blocks // qc
        qk = blocks % qc
        piece = SOURCE // qc

        own = spectra.reshape(qc, piece, windows, width)
        by_off = [lax.dynamic_index_in_dim(own, q, 0, keepdims=False)]
        for d in range(1, qc):
            send = lax.dynamic_index_in_dim(own, q ^ d, 0, keepdims=False)
            by_off.append(
                lax.ppermute(send, "chan", pairs_of(n, lambda i, d=d: (i // qc) * qc + ((i % qc) ^ d)))
            )
        by_off = jnp.stack(by_off)

        here = zk == z
        sel = jnp.take(by_off, qk ^ q, axis=0)
        payload = jnp.where(here[:, None, None, None], sel, jnp.zeros_like(sel))

        up_pairs = pairs_of(n, lambda i: i + qc if i // qc < zc - 1 else None)
        down_pairs = pairs_of(n, lambda i: i - qc if i // qc > 0 else None)
        mask = here[:, None, None, None]
        cur_up, cur_down = payload, payload
        rec_up, rec_down = payload, payload
        for r in range(zc - 1):
            rec_up = lax.ppermute(cur_up, "chan", up_pairs)
            rec_down = lax.ppermute(cur_down, "chan", down_pairs)
            if r < zc - 2:
                cur_up = jnp.where(mask, payload, rec_up)
                cur_down = jnp.where(mask, payload, rec_down)
        below = (z > zk)[:, None, None, None]
        mine = jnp.where(mask, payload, jnp.where(below, rec_up, rec_down))

        offs = [0]
        held = [mine]
        for b in plane_bits:
            got = lax.ppermute(
                jnp.stack(held), "chan", pairs_of(n, lambda i, b=b: (i // qc) * qc + ((i % qc) ^ b))
            )
            offs = offs + [o ^ b for o in offs]
            held = held + [got[i] for i in range(got.shape[0])]
        stack = jnp.stack(held)
        inv = [0] * qc
        for e, o in enumerate(offs):
            inv[o] = e
        inv = jnp.array(inv, jnp.int32)
        order = jnp.take(inv, jnp.arange(qc, dtype=jnp.int32) ^ q)
        full = jnp.take(stack, order, axis=0)
        src_all = jnp.transpose(full, (1, 0, 2, 3, 4)).reshape(nb, SOURCE, windows, width)

        lag_table = build_table(bins, LAGS)
        window_mask = window_valid.astype(jnp.bfloat16)[None, None, :, None]
        src_all = src_all * window_mask
        cross = cross_products(src_all, spectra)
        traces = jnp.dot(
            cross.reshape(nb * SOURCE * receivers, width), lag_table, preferred_element_type=jnp.float32
        ).reshape(nb, SOURCE, receivers, LAGS)
        traces_all = [traces[k] for k in range(nb)]
        peaks = [jnp.max(jnp.abs(traces[k]), axis=(1, 2)) for k in range(nb)]
        peak = jnp.stack(peaks)
        d = 1
        while d < n:
            peak = jnp.maximum(peak, lax.ppermute(peak, "chan", pairs_of(n, lambda i, d=d: i ^ d)))
            d *= 2
        out = [
            (traces_all[k] / (peak[k][:, None, None] + 1e-06)).astype(jnp.bfloat16) for k in range(nb)
        ]
        stacked = jnp.stack(out, axis=0)
        return stacked.reshape(source_blocks.shape[0], source_blocks.shape[1], SOURCE, receivers, LAGS)

    return shards


def solution(mesh):
    n = mesh.shape["chan"]
    qc = plane_size(mesh)
    placed = (P(("parts", "chan"), None, None), P("parts", None), P("parts"))
    return jax.shard_map(
        make_shards(n, qc),
        mesh=mesh,
        in_specs=placed,
        out_specs=P(None, None, None, ("parts", "chan"), None),
        check_vma=False,
    )
```

```python
import math

import jax
import ml_dtypes
import numpy as np
import jax.numpy as jnp
from jax import lax
from jax.experimental import pallas as pl
from jax.experimental.pallas import tpu as pltpu
from jax.sharding import PartitionSpec as P

SOURCE = 32
LAGS = 512


def build_table(bins, lags):
    freq = np.arange(bins, dtype=np.int32)[:, None]
    shifted = np.arange(lags, dtype=np.int32)[None, :] - lags // 2
    phase = np.remainder(freq * shifted, 2 * bins).astype(np.float32)
    theta = phase * np.float32(2.0 * math.pi / (2 * bins))
    weight = (np.where(freq == 0, 1.0, 2.0).astype(np.float32) / np.float32(2 * bins)).astype(np.float32)
    table = np.concatenate([weight * np.cos(theta), -weight * np.sin(theta)], axis=0).astype(np.float32)
    return jnp.asarray(table.astype(ml_dtypes.bfloat16))


ST = 8
RC = 16


def cross_kernel(order_ref, src_ref, rcv_ref, out_ref):
    del order_ref
    bins = src_ref.shape[-1] // 2
    windows = src_ref.shape[3]
    rows = rcv_ref.shape[1]

    def body(s, carry):
        row = src_ref[0, 0, s].astype(jnp.float32)
        for c in range(rows // RC):
            rs = slice(c * RC, (c + 1) * RC)
            acc_re = jnp.zeros((RC, bins), jnp.float32)
            acc_im = jnp.zeros((RC, bins), jnp.float32)
            for w in range(windows):
                a = jnp.broadcast_to(row[w : w + 1, :bins], (RC, bins))
                b = jnp.broadcast_to(row[w : w + 1, bins:], (RC, bins))
                rr = rcv_ref[w, rs, :bins]
                ri = rcv_ref[w, rs, bins:]
                acc_re = acc_re + (a * rr + b * ri)
                acc_im = acc_im + (a * ri - b * rr)
            out_ref[0, s, rs, :bins] = acc_re.astype(out_ref.dtype)
            out_ref[0, s, rs, bins:] = acc_im.astype(out_ref.dtype)
        return carry

    lax.fori_loop(0, src_ref.shape[2], body, 0)


def cross_products(stack, order, rcv_t):
    qc, nb, piece, windows, width = stack.shape
    receivers = rcv_t.shape[1]
    sources = qc * piece
    flops = 8 * nb * sources * receivers * windows * (width // 2)
    return pl.pallas_call(
        cross_kernel,
        grid_spec=pltpu.PrefetchScalarGridSpec(
            num_scalar_prefetch=1,
            grid=(nb, qc),
            in_specs=[
                pl.BlockSpec((1, 1, piece, windows, width), lambda k, i, o: (o[i], k, 0, 0, 0)),
                pl.BlockSpec((windows, receivers, width), lambda k, i, o: (0, 0, 0)),
            ],
            out_specs=pl.BlockSpec((1, piece, receivers, width), lambda k, i, o: (k, i, 0, 0)),
        ),
        out_shape=jax.ShapeDtypeStruct((nb, sources, receivers, width), jnp.bfloat16),
        cost_estimate=pl.CostEstimate(
            flops=flops,
            bytes_accessed=stack.size * 2 + rcv_t.size * 4 + nb * sources * receivers * width * 2,
            transcendentals=0,
        ),
    )(order, stack, rcv_t)

def plane_size(mesh):
    devs = list(mesh.devices[0])
    n = len(devs)
    best = 1
    for axis in range(3):
        first = next((i for i, d in enumerate(devs) if d.coords[axis] != devs[0].coords[axis]), None)
        if first is not None and first > best:
            best = first
    if best >= n or n % best:
        best = 1
    return best


def pairs_of(n, fn):
    out = []
    for i in range(n):
        j = fn(i)
        if j is not None:
            out.append((i, j))
    return out


def make_shards(n, qc):
    zc = n // qc
    plane_bits = [1 << b for b in reversed(range(qc.bit_length() - 1))]

    def shards(spectra, source_blocks, window_valid):
        receivers, windows, width = spectra.shape
        bins = width // 2
        me = lax.axis_index("chan")
        z = me // qc
        q = me % qc
        blocks = source_blocks.reshape(-1)
        nb = blocks.shape[0]
        zk = blocks // qc
        qk = blocks % qc
        piece = SOURCE // qc

        own = spectra.reshape(qc, piece, windows, width)
        by_off = [lax.dynamic_index_in_dim(own, q, 0, keepdims=False)]
        for d in range(1, qc):
            send = lax.dynamic_index_in_dim(own, q ^ d, 0, keepdims=False)
            by_off.append(
                lax.ppermute(send, "chan", pairs_of(n, lambda i, d=d: (i // qc) * qc + ((i % qc) ^ d)))
            )
        by_off = jnp.stack(by_off)

        here = zk == z
        sel = jnp.take(by_off, qk ^ q, axis=0)
        payload = jnp.where(here[:, None, None, None], sel, jnp.zeros_like(sel))

        up_pairs = pairs_of(n, lambda i: i + qc if i // qc < zc - 1 else None)
        down_pairs = pairs_of(n, lambda i: i - qc if i // qc > 0 else None)
        mask = here[:, None, None, None]
        cur_up, cur_down = payload, payload
        rec_up, rec_down = payload, payload
        for r in range(zc - 1):
            rec_up = lax.ppermute(cur_up, "chan", up_pairs)
            rec_down = lax.ppermute(cur_down, "chan", down_pairs)
            if r < zc - 2:
                cur_up = jnp.where(mask, payload, rec_up)
                cur_down = jnp.where(mask, payload, rec_down)
        below = (z > zk)[:, None, None, None]
        mine = jnp.where(mask, payload, jnp.where(below, rec_up, rec_down))

        offs = [0]
        held = [mine]
        for b in plane_bits:
            got = lax.ppermute(
                jnp.stack(held), "chan", pairs_of(n, lambda i, b=b: (i // qc) * qc + ((i % qc) ^ b))
            )
            offs = offs + [o ^ b for o in offs]
            held = held + [got[i] for i in range(got.shape[0])]
        stack = jnp.stack(held)
        inv = [0] * qc
        for e, o in enumerate(offs):
            inv[o] = e
        order = jnp.take(jnp.array(inv, jnp.int32), jnp.arange(qc, dtype=jnp.int32) ^ q)

        lag_table = build_table(bins, LAGS)
        window_mask = window_valid.astype(jnp.float32)[:, None, None]
        rcv_t = jnp.transpose(spectra, (1, 0, 2)).astype(jnp.float32) * window_mask
        cross = cross_products(stack, order, rcv_t)
        traces = jnp.dot(
            cross.reshape(nb * SOURCE * receivers, width), lag_table, preferred_element_type=jnp.float32
        ).reshape(nb, SOURCE, receivers, LAGS)
        traces_all = [traces[k] for k in range(nb)]
        peaks = [jnp.max(jnp.abs(traces[k]), axis=(1, 2)) for k in range(nb)]
        peak = jnp.stack(peaks)
        got = [
            lax.ppermute(peak, "chan", pairs_of(n, lambda i, d=d: (i // qc) * qc + ((i % qc) ^ d)))
            for d in range(1, qc)
        ]
        for g in got:
            peak = jnp.maximum(peak, g)
        got = [
            lax.ppermute(peak, "chan", pairs_of(n, lambda i, d=d: ((i // qc + d) % zc) * qc + i % qc))
            for d in range(1, zc)
        ]
        for g in got:
            peak = jnp.maximum(peak, g)
        out = [
            (traces_all[k] / (peak[k][:, None, None] + 1e-06)).astype(jnp.bfloat16) for k in range(nb)
        ]
        stacked = jnp.stack(out, axis=0)
        return stacked.reshape(source_blocks.shape[0], source_blocks.shape[1], SOURCE, receivers, LAGS)

    return shards


def solution(mesh):
    n = mesh.shape["chan"]
    qc = plane_size(mesh)
    placed = (P(("parts", "chan"), None, None), P("parts", None), P("parts"))
    return jax.shard_map(
        make_shards(n, qc),
        mesh=mesh,
        in_specs=placed,
        out_specs=P(None, None, None, ("parts", "chan"), None),
        check_vma=False,
    )
```

```python
import math

import jax
import ml_dtypes
import numpy as np
import jax.numpy as jnp
from jax import lax
from jax.experimental import pallas as pl
from jax.experimental.pallas import tpu as pltpu
from jax.sharding import PartitionSpec as P

SOURCE = 32
LAGS = 512


def build_table(bins, lags):
    freq = np.arange(bins, dtype=np.int32)[:, None]
    shifted = np.arange(lags, dtype=np.int32)[None, :] - lags // 2
    phase = np.remainder(freq * shifted, 2 * bins).astype(np.float32)
    theta = phase * np.float32(2.0 * math.pi / (2 * bins))
    weight = (np.where(freq == 0, 1.0, 2.0).astype(np.float32) / np.float32(2 * bins)).astype(np.float32)
    table = np.concatenate([weight * np.cos(theta), -weight * np.sin(theta)], axis=0).astype(np.float32)
    return jnp.asarray(table.astype(ml_dtypes.bfloat16))


ST = 8
RC = 16


def cross_kernel(order_ref, src_ref, rcv_ref, out_ref):
    del order_ref
    bins = src_ref.shape[-1] // 2
    windows = src_ref.shape[3]
    rows = rcv_ref.shape[1]

    def body(s, carry):
        row = src_ref[0, 0, s].astype(jnp.float32)
        for c in range(rows // RC):
            rs = slice(c * RC, (c + 1) * RC)
            acc_re = jnp.zeros((RC, bins), jnp.float32)
            acc_im = jnp.zeros((RC, bins), jnp.float32)
            for w in range(windows):
                a = jnp.broadcast_to(row[w : w + 1, :bins], (RC, bins))
                b = jnp.broadcast_to(row[w : w + 1, bins:], (RC, bins))
                rr = rcv_ref[w, rs, :bins]
                ri = rcv_ref[w, rs, bins:]
                acc_re = acc_re + (a * rr + b * ri)
                acc_im = acc_im + (a * ri - b * rr)
            out_ref[0, s, rs, :bins] = acc_re.astype(out_ref.dtype)
            out_ref[0, s, rs, bins:] = acc_im.astype(out_ref.dtype)
        return carry

    lax.fori_loop(0, src_ref.shape[2], body, 0)


def cross_products(stack, order, rcv_t):
    qc, nb, piece, windows, width = stack.shape
    receivers = rcv_t.shape[1]
    sources = qc * piece
    flops = 8 * nb * sources * receivers * windows * (width // 2)
    return pl.pallas_call(
        cross_kernel,
        grid_spec=pltpu.PrefetchScalarGridSpec(
            num_scalar_prefetch=1,
            grid=(nb, qc),
            in_specs=[
                pl.BlockSpec((1, 1, piece, windows, width), lambda k, i, o: (o[i], k, 0, 0, 0)),
                pl.BlockSpec((windows, receivers, width), lambda k, i, o: (0, 0, 0)),
            ],
            out_specs=pl.BlockSpec((1, piece, receivers, width), lambda k, i, o: (k, i, 0, 0)),
        ),
        out_shape=jax.ShapeDtypeStruct((nb, sources, receivers, width), jnp.bfloat16),
        cost_estimate=pl.CostEstimate(
            flops=flops,
            bytes_accessed=stack.size * 2 + rcv_t.size * 4 + nb * sources * receivers * width * 2,
            transcendentals=0,
        ),
    )(order, stack, rcv_t)

def plane_size(mesh):
    devs = list(mesh.devices[0])
    n = len(devs)
    best = 1
    for axis in range(3):
        first = next((i for i, d in enumerate(devs) if d.coords[axis] != devs[0].coords[axis]), None)
        if first is not None and first > best:
            best = first
    if best >= n or n % best:
        best = 1
    return best


def pairs_of(n, fn):
    out = []
    for i in range(n):
        j = fn(i)
        if j is not None:
            out.append((i, j))
    return out


def make_shards(n, qc):
    zc = n // qc
    plane_bits = [1 << b for b in reversed(range(qc.bit_length() - 1))]

    def shards(spectra, source_blocks, window_valid):
        receivers, windows, width = spectra.shape
        bins = width // 2
        me = lax.axis_index("chan")
        z = me // qc
        q = me % qc
        blocks = source_blocks.reshape(-1)
        nb = blocks.shape[0]
        zk = blocks // qc
        qk = blocks % qc
        piece = SOURCE // qc

        own = spectra.reshape(qc, piece, windows, width)
        by_off = [lax.dynamic_index_in_dim(own, q, 0, keepdims=False)]
        for d in range(1, qc):
            send = lax.dynamic_index_in_dim(own, q ^ d, 0, keepdims=False)
            by_off.append(
                lax.ppermute(send, "chan", pairs_of(n, lambda i, d=d: (i // qc) * qc + ((i % qc) ^ d)))
            )
        by_off = jnp.stack(by_off)

        here = zk == z
        sel = jnp.take(by_off, qk ^ q, axis=0)
        payload = jnp.where(here[:, None, None, None], sel, jnp.zeros_like(sel))

        mask = here[:, None, None, None]
        if zc & (zc - 1) == 0:
            mine = payload
            d = 1
            while d < zc:
                got = lax.ppermute(mine, "chan", pairs_of(n, lambda i, d=d: (((i // qc) ^ d) * qc) + i % qc))
                valid = (((zk ^ z) & ~(d - 1)) == 0)[:, None, None, None]
                mine = jnp.where(valid, mine, got)
                d *= 2
        else:
            up_pairs = pairs_of(n, lambda i: i + qc if i // qc < zc - 1 else None)
            down_pairs = pairs_of(n, lambda i: i - qc if i // qc > 0 else None)
            cur_up, cur_down = payload, payload
            rec_up, rec_down = payload, payload
            for r in range(zc - 1):
                rec_up = lax.ppermute(cur_up, "chan", up_pairs)
                rec_down = lax.ppermute(cur_down, "chan", down_pairs)
                if r < zc - 2:
                    cur_up = jnp.where(mask, payload, rec_up)
                    cur_down = jnp.where(mask, payload, rec_down)
            below = (z > zk)[:, None, None, None]
            mine = jnp.where(mask, payload, jnp.where(below, rec_up, rec_down))

        offs = [0]
        held = [mine]
        for b in plane_bits:
            got = lax.ppermute(
                jnp.stack(held), "chan", pairs_of(n, lambda i, b=b: (i // qc) * qc + ((i % qc) ^ b))
            )
            offs = offs + [o ^ b for o in offs]
            held = held + [got[i] for i in range(got.shape[0])]
        stack = jnp.stack(held)
        inv = [0] * qc
        for e, o in enumerate(offs):
            inv[o] = e
        order = jnp.take(jnp.array(inv, jnp.int32), jnp.arange(qc, dtype=jnp.int32) ^ q)

        lag_table = build_table(bins, LAGS)
        window_mask = window_valid.astype(jnp.float32)[:, None, None]
        rcv_t = jnp.transpose(spectra, (1, 0, 2)).astype(jnp.float32) * window_mask
        cross = cross_products(stack, order, rcv_t)
        traces = jnp.dot(
            cross.reshape(nb * SOURCE * receivers, width), lag_table, preferred_element_type=jnp.float32
        ).reshape(nb, SOURCE, receivers, LAGS)
        peak = jnp.max(jnp.abs(traces), axis=(2, 3))
        got = [
            lax.ppermute(peak, "chan", pairs_of(n, lambda i, d=d: (i // qc) * qc + ((i % qc) ^ d)))
            for d in range(1, qc)
        ]
        for g in got:
            peak = jnp.maximum(peak, g)
        got = [
            lax.ppermute(peak, "chan", pairs_of(n, lambda i, d=d: ((i // qc + d) % zc) * qc + i % qc))
            for d in range(1, zc)
        ]
        for g in got:
            peak = jnp.maximum(peak, g)
        normed = (traces / (peak[:, :, None, None] + 1e-06)).astype(jnp.bfloat16)
        return normed.reshape(source_blocks.shape[0], source_blocks.shape[1], SOURCE, receivers, LAGS)

    return shards


def solution(mesh):
    n = mesh.shape["chan"]
    qc = plane_size(mesh)
    placed = (P(("parts", "chan"), None, None), P("parts", None), P("parts"))
    return jax.shard_map(
        make_shards(n, qc),
        mesh=mesh,
        in_specs=placed,
        out_specs=P(None, None, None, ("parts", "chan"), None),
        check_vma=False,
    )
```

```python
import math

import jax
import ml_dtypes
import numpy as np
import jax.numpy as jnp
from jax import lax
from jax.experimental import pallas as pl
from jax.experimental.pallas import tpu as pltpu
from jax.sharding import PartitionSpec as P


SOURCE = 32
LAGS = 512


def build_table(bins, lags):
    freq = np.arange(bins, dtype=np.int32)[:, None]
    shifted = np.arange(lags, dtype=np.int32)[None, :] - lags // 2
    phase = np.remainder(freq * shifted, 2 * bins).astype(np.float32)
    theta = phase * np.float32(2.0 * math.pi / (2 * bins))
    weight = (np.where(freq == 0, 1.0, 2.0).astype(np.float32) / np.float32(2 * bins)).astype(np.float32)
    table = np.concatenate([weight * np.cos(theta), -weight * np.sin(theta)], axis=0).astype(np.float32)
    return jnp.asarray(table.astype(ml_dtypes.bfloat16))


RC = 16


def cross_kernel(pos_ref, src_ref, rcv_ref, *rest):
    del pos_ref
    out_ref = rest[-1]
    bins = src_ref.shape[-1] // 2
    windows = src_ref.shape[3]
    rows = rcv_ref.shape[1]

    def body(s, carry):
        row = src_ref[0, 0, s].astype(jnp.float32)
        for c in range(rows // RC):
            rs = slice(c * RC, (c + 1) * RC)
            acc_re = jnp.zeros((RC, bins), jnp.float32)
            acc_im = jnp.zeros((RC, bins), jnp.float32)
            for w in range(windows):
                a = jnp.broadcast_to(row[w : w + 1, :bins], (RC, bins))
                b = jnp.broadcast_to(row[w : w + 1, bins:], (RC, bins))
                rr = rcv_ref[w, rs, :bins]
                ri = rcv_ref[w, rs, bins:]
                acc_re = acc_re + (a * rr + b * ri)
                acc_im = acc_im + (a * ri - b * rr)
            out_ref[0, s, rs, :bins] = acc_re.astype(out_ref.dtype)
            out_ref[0, s, rs, bins:] = acc_im.astype(out_ref.dtype)
        return carry

    lax.fori_loop(0, src_ref.shape[2], body, 0)


def cross_part(entries, pos, rcv_t, buf=None):
    m, nb, piece, windows, width = entries.shape
    receivers = rcv_t.shape[1]
    qc = SOURCE // piece
    flops = 8 * nb * m * piece * receivers * windows * (width // 2)
    in_specs = [
        pl.BlockSpec((1, 1, piece, windows, width), lambda k, i, o: (i, k, 0, 0, 0)),
        pl.BlockSpec((windows, receivers, width), lambda k, i, o: (0, 0, 0)),
    ]
    args = [pos, entries, rcv_t]
    aliases = {}
    if buf is not None:
        in_specs.append(pl.BlockSpec(memory_space=pl.ANY))
        args.append(buf)
        aliases = {3: 0}
    return pl.pallas_call(
        cross_kernel,
        grid_spec=pltpu.PrefetchScalarGridSpec(
            num_scalar_prefetch=1,
            grid=(nb, m),
            in_specs=in_specs,
            out_specs=pl.BlockSpec((1, piece, receivers, width), lambda k, i, o: (k, o[i], 0, 0)),
        ),
        out_shape=jax.ShapeDtypeStruct((nb, qc * piece, receivers, width), jnp.bfloat16),
        input_output_aliases=aliases,
        cost_estimate=pl.CostEstimate(
            flops=flops,
            bytes_accessed=entries.size * 2 + rcv_t.size * 4 + nb * m * piece * receivers * width * 2,
            transcendentals=0,
        ),
    )(*args)


def plane_size(mesh):
    devs = list(mesh.devices[0])
    n = len(devs)
    best = 1
    for axis in range(3):
        first = next((i for i, d in enumerate(devs) if d.coords[axis] != devs[0].coords[axis]), None)
        if first is not None and first > best:
            best = first
    if best >= n or n % best:
        best = 1
    return best


def pairs_of(n, fn):
    out = []
    for i in range(n):
        j = fn(i)
        if j is not None:
            out.append((i, j))
    return out


def make_shards(n, qc):
    zc = n // qc
    plane_bits = [1 << b for b in reversed(range(qc.bit_length() - 1))]

    def shards(spectra, source_blocks, window_valid):
        receivers, windows, width = spectra.shape
        bins = width // 2
        me = lax.axis_index("chan")
        z = me // qc
        q = me % qc
        blocks = source_blocks.reshape(-1)
        nb = blocks.shape[0]
        zk = blocks // qc
        qk = blocks % qc
        piece = SOURCE // qc

        own = spectra.reshape(qc, piece, windows, width)
        by_off = [lax.dynamic_index_in_dim(own, q, 0, keepdims=False)]
        for d in range(1, qc):
            send = lax.dynamic_index_in_dim(own, q ^ d, 0, keepdims=False)
            by_off.append(
                lax.ppermute(send, "chan", pairs_of(n, lambda i, d=d: (i // qc) * qc + ((i % qc) ^ d)))
            )
        by_off = jnp.stack(by_off)

        here = zk == z
        sel = jnp.take(by_off, qk ^ q, axis=0)
        payload = jnp.where(here[:, None, None, None], sel, jnp.zeros_like(sel))

        mask = here[:, None, None, None]
        if zc & (zc - 1) == 0:
            mine = payload
            d = 1
            while d < zc:
                got = lax.ppermute(mine, "chan", pairs_of(n, lambda i, d=d: (((i // qc) ^ d) * qc) + i % qc))
                valid = (((zk ^ z) & ~(d - 1)) == 0)[:, None, None, None]
                mine = jnp.where(valid, mine, got)
                d *= 2
        else:
            up_pairs = pairs_of(n, lambda i: i + qc if i // qc < zc - 1 else None)
            down_pairs = pairs_of(n, lambda i: i - qc if i // qc > 0 else None)
            cur_up, cur_down = payload, payload
            rec_up, rec_down = payload, payload
            for r in range(zc - 1):
                rec_up = lax.ppermute(cur_up, "chan", up_pairs)
                rec_down = lax.ppermute(cur_down, "chan", down_pairs)
                if r < zc - 2:
                    cur_up = jnp.where(mask, payload, rec_up)
                    cur_down = jnp.where(mask, payload, rec_down)
            below = (z > zk)[:, None, None, None]
            mine = jnp.where(mask, payload, jnp.where(below, rec_up, rec_down))

        lag_table = build_table(bins, LAGS)
        window_mask = window_valid.astype(jnp.float32)[:, None, None]
        rcv_t = jnp.transpose(spectra, (1, 0, 2)).astype(jnp.float32) * window_mask

        cross = cross_part(mine[None], q[None].astype(jnp.int32), rcv_t)
        offs = [0]
        held = [mine]
        for b in plane_bits:
            got = lax.ppermute(
                jnp.stack(held), "chan", pairs_of(n, lambda i, b=b: (i // qc) * qc + ((i % qc) ^ b))
            )
            new_offs = [o ^ b for o in offs]
            pos = q ^ jnp.array(new_offs, jnp.int32)
            cross = cross_part(got, pos, rcv_t, cross)
            offs = offs + new_offs
            held = held + [got[i] for i in range(got.shape[0])]
        traces = jnp.dot(
            cross.reshape(nb * SOURCE * receivers, width), lag_table, preferred_element_type=jnp.float32
        ).reshape(nb, SOURCE, receivers, LAGS)
        peak = jnp.max(jnp.abs(traces), axis=(2, 3))
        got = [
            lax.ppermute(peak, "chan", pairs_of(n, lambda i, d=d: (i // qc) * qc + ((i % qc) ^ d)))
            for d in range(1, qc)
        ]
        for g in got:
            peak = jnp.maximum(peak, g)
        got = [
            lax.ppermute(peak, "chan", pairs_of(n, lambda i, d=d: ((i // qc + d) % zc) * qc + i % qc))
            for d in range(1, zc)
        ]
        for g in got:
            peak = jnp.maximum(peak, g)
        normed = (traces / (peak[:, :, None, None] + 1e-06)).astype(jnp.bfloat16)
        return normed.reshape(source_blocks.shape[0], source_blocks.shape[1], SOURCE, receivers, LAGS)

    return shards


def solution(mesh):
    n = mesh.shape["chan"]
    qc = plane_size(mesh)
    placed = (P(("parts", "chan"), None, None), P("parts", None), P("parts"))
    inner = make_shards(n, qc)

    return jax.shard_map(
        inner,
        mesh=mesh,
        in_specs=placed,
        out_specs=P(None, None, None, ("parts", "chan"), None),
        check_vma=False,
    )
```

```python
import math

import jax
import ml_dtypes
import numpy as np
import jax.numpy as jnp
from jax import lax
from jax.experimental import pallas as pl
from jax.experimental.pallas import tpu as pltpu
from jax.sharding import PartitionSpec as P


SOURCE = 32
LAGS = 512


def build_table(bins, lags):
    freq = np.arange(bins, dtype=np.int32)[:, None]
    shifted = np.arange(lags, dtype=np.int32)[None, :] - lags // 2
    phase = np.remainder(freq * shifted, 2 * bins).astype(np.float32)
    theta = phase * np.float32(2.0 * math.pi / (2 * bins))
    weight = (np.where(freq == 0, 1.0, 2.0).astype(np.float32) / np.float32(2 * bins)).astype(np.float32)
    table = np.concatenate([weight * np.cos(theta), -weight * np.sin(theta)], axis=0).astype(np.float32)
    return jnp.asarray(table.astype(ml_dtypes.bfloat16))


RC = 16


def cross_kernel(pos_ref, src_ref, rcv_ref, *rest):
    del pos_ref
    out_ref = rest[-1]
    bins = src_ref.shape[-1] // 2
    windows = src_ref.shape[3]
    rows = rcv_ref.shape[2]

    def body(s, carry):
        row = src_ref[0, 0, s].astype(jnp.float32)
        for c in range(rows // RC):
            rs = slice(c * RC, (c + 1) * RC)
            acc1 = jnp.zeros((RC, bins), jnp.float32)
            acc2 = jnp.zeros((RC, bins), jnp.float32)
            acc3 = jnp.zeros((RC, bins), jnp.float32)
            for w in range(windows):
                a = row[w : w + 1, :bins]
                b = row[w : w + 1, bins:]
                amb = jnp.broadcast_to(a - b, (RC, bins))
                a = jnp.broadcast_to(a, (RC, bins))
                b = jnp.broadcast_to(b, (RC, bins))
                acc1 = acc1 + rcv_ref[0, w, rs, :] * amb
                acc2 = acc2 + rcv_ref[1, w, rs, :] * a
                acc3 = acc3 + rcv_ref[2, w, rs, :] * b
            out_ref[0, s, rs, :bins] = (acc1 + acc3).astype(out_ref.dtype)
            out_ref[0, s, rs, bins:] = (acc1 + acc2).astype(out_ref.dtype)
        return carry

    lax.fori_loop(0, src_ref.shape[2], body, 0)


def cross_part(entries, pos, rcv_t, buf=None):
    m, nb, piece, windows, width = entries.shape
    receivers = rcv_t.shape[2]
    qc = SOURCE // piece
    flops = 6 * nb * m * piece * receivers * windows * (width // 2)
    in_specs = [
        pl.BlockSpec((1, 1, piece, windows, width), lambda k, i, o: (i, k, 0, 0, 0)),
        pl.BlockSpec((3, windows, receivers, width // 2), lambda k, i, o: (0, 0, 0, 0)),
    ]
    args = [pos, entries, rcv_t]
    aliases = {}
    if buf is not None:
        in_specs.append(pl.BlockSpec(memory_space=pl.ANY))
        args.append(buf)
        aliases = {3: 0}
    return pl.pallas_call(
        cross_kernel,
        grid_spec=pltpu.PrefetchScalarGridSpec(
            num_scalar_prefetch=1,
            grid=(nb, m),
            in_specs=in_specs,
            out_specs=pl.BlockSpec((1, piece, receivers, width), lambda k, i, o: (k, o[i], 0, 0)),
        ),
        out_shape=jax.ShapeDtypeStruct((nb, qc * piece, receivers, width), jnp.bfloat16),
        input_output_aliases=aliases,
        cost_estimate=pl.CostEstimate(
            flops=flops,
            bytes_accessed=entries.size * 2 + rcv_t.size * 4 + nb * m * piece * receivers * width * 2,
            transcendentals=0,
        ),
    )(*args)


def plane_size(mesh):
    devs = list(mesh.devices[0])
    n = len(devs)
    best = 1
    for axis in range(3):
        first = next((i for i, d in enumerate(devs) if d.coords[axis] != devs[0].coords[axis]), None)
        if first is not None and first > best:
            best = first
    if best >= n or n % best:
        best = 1
    return best


def pairs_of(n, fn):
    out = []
    for i in range(n):
        j = fn(i)
        if j is not None:
            out.append((i, j))
    return out


def make_shards(n, qc):
    zc = n // qc
    plane_bits = [1 << b for b in reversed(range(qc.bit_length() - 1))]

    def shards(spectra, source_blocks, window_valid):
        receivers, windows, width = spectra.shape
        bins = width // 2
        me = lax.axis_index("chan")
        z = me // qc
        q = me % qc
        blocks = source_blocks.reshape(-1)
        nb = blocks.shape[0]
        zk = blocks // qc
        qk = blocks % qc
        piece = SOURCE // qc

        own = spectra.reshape(qc, piece, windows, width)
        by_off = [lax.dynamic_index_in_dim(own, q, 0, keepdims=False)]
        for d in range(1, qc):
            send = lax.dynamic_index_in_dim(own, q ^ d, 0, keepdims=False)
            by_off.append(
                lax.ppermute(send, "chan", pairs_of(n, lambda i, d=d: (i // qc) * qc + ((i % qc) ^ d)))
            )
        by_off = jnp.stack(by_off)

        here = zk == z
        sel = jnp.take(by_off, qk ^ q, axis=0)
        payload = jnp.where(here[:, None, None, None], sel, jnp.zeros_like(sel))

        mask = here[:, None, None, None]
        if zc & (zc - 1) == 0:
            mine = payload
            d = 1
            while d < zc:
                got = lax.ppermute(
                    mine, "chan", pairs_of(n, lambda i, d=d: (((i // qc) ^ d) * qc) + i % qc)
                )
                valid = (((zk ^ z) & ~(d - 1)) == 0)[:, None, None, None]
                mine = jnp.where(valid, mine, got)
                d *= 2
        else:
            up_pairs = pairs_of(n, lambda i: i + qc if i // qc < zc - 1 else None)
            down_pairs = pairs_of(n, lambda i: i - qc if i // qc > 0 else None)
            cur_up, cur_down = payload, payload
            rec_up, rec_down = payload, payload
            for r in range(zc - 1):
                rec_up = lax.ppermute(cur_up, "chan", up_pairs)
                rec_down = lax.ppermute(cur_down, "chan", down_pairs)
                if r < zc - 2:
                    cur_up = jnp.where(mask, payload, rec_up)
                    cur_down = jnp.where(mask, payload, rec_down)
            below = (z > zk)[:, None, None, None]
            mine = jnp.where(mask, payload, jnp.where(below, rec_up, rec_down))

        lag_table = build_table(bins, LAGS)
        window_mask = window_valid.astype(jnp.float32)[:, None, None]
        rcv_t = jnp.transpose(spectra, (1, 0, 2)).astype(jnp.float32) * window_mask
        rc, rd = rcv_t[..., :bins], rcv_t[..., bins:]
        rcv_t = jnp.stack([rc, rd - rc, rc + rd])

        cross = cross_part(mine[None], q[None].astype(jnp.int32), rcv_t)
        offs = [0]
        held = [mine]
        for b in plane_bits:
            got = lax.ppermute(
                jnp.stack(held), "chan", pairs_of(n, lambda i, b=b: (i // qc) * qc + ((i % qc) ^ b))
            )
            new_offs = [o ^ b for o in offs]
            pos = q ^ jnp.array(new_offs, jnp.int32)
            cross = cross_part(got, pos, rcv_t, cross)
            offs = offs + new_offs
            held = held + [got[i] for i in range(got.shape[0])]
        traces = jnp.dot(
            cross.reshape(nb * SOURCE * receivers, width), lag_table, preferred_element_type=jnp.float32
        ).reshape(nb, SOURCE, receivers, LAGS)
        peak = jnp.max(jnp.abs(traces), axis=(2, 3))
        got = [
            lax.ppermute(peak, "chan", pairs_of(n, lambda i, d=d: (i // qc) * qc + ((i % qc) ^ d)))
            for d in range(1, qc)
        ]
        for g in got:
            peak = jnp.maximum(peak, g)
        got = [
            lax.ppermute(peak, "chan", pairs_of(n, lambda i, d=d: ((i // qc + d) % zc) * qc + i % qc))
            for d in range(1, zc)
        ]
        for g in got:
            peak = jnp.maximum(peak, g)
        normed = (traces / (peak[:, :, None, None] + 1e-06)).astype(jnp.bfloat16)
        return normed.reshape(source_blocks.shape[0], source_blocks.shape[1], SOURCE, receivers, LAGS)

    return shards


def solution(mesh):
    n = mesh.shape["chan"]
    qc = plane_size(mesh)
    placed = (P(("parts", "chan"), None, None), P("parts", None), P("parts"))
    inner = make_shards(n, qc)

    return jax.shard_map(
        inner,
        mesh=mesh,
        in_specs=placed,
        out_specs=P(None, None, None, ("parts", "chan"), None),
        check_vma=False,
    )
```

```python
import math

import jax
import ml_dtypes
import numpy as np
import jax.numpy as jnp
from jax import lax
from jax.experimental import pallas as pl
from jax.experimental.pallas import tpu as pltpu
from jax.sharding import PartitionSpec as P


SOURCE = 32
LAGS = 512


def build_table(bins, lags):
    freq = np.arange(bins, dtype=np.int32)[:, None]
    shifted = np.arange(lags, dtype=np.int32)[None, :] - lags // 2
    phase = np.remainder(freq * shifted, 2 * bins).astype(np.float32)
    theta = phase * np.float32(2.0 * math.pi / (2 * bins))
    weight = (np.where(freq == 0, 1.0, 2.0).astype(np.float32) / np.float32(2 * bins)).astype(np.float32)
    table = np.concatenate([weight * np.cos(theta), -weight * np.sin(theta)], axis=0).astype(np.float32)
    return jnp.asarray(table.astype(ml_dtypes.bfloat16))


RC = 16


def cross_kernel(pos_ref, src_ref, rcv_ref, *rest):
    del pos_ref
    out_ref = rest[-1]
    bins = src_ref.shape[-1] // 2
    windows = src_ref.shape[3]
    rows = rcv_ref.shape[2]

    def body(s, carry):
        row = src_ref[0, 0, s].astype(jnp.float32)
        for c in range(rows // RC):
            rs = slice(c * RC, (c + 1) * RC)
            acc1 = jnp.zeros((RC, bins), jnp.float32)
            acc2 = jnp.zeros((RC, bins), jnp.float32)
            acc3 = jnp.zeros((RC, bins), jnp.float32)
            for w in range(windows):
                a = row[w : w + 1, :bins]
                b = row[w : w + 1, bins:]
                amb = jnp.broadcast_to(a - b, (RC, bins))
                a = jnp.broadcast_to(a, (RC, bins))
                b = jnp.broadcast_to(b, (RC, bins))
                acc1 = acc1 + rcv_ref[0, w, rs, :] * amb
                acc2 = acc2 + rcv_ref[1, w, rs, :] * a
                acc3 = acc3 + rcv_ref[2, w, rs, :] * b
            out_ref[0, s, rs, :bins] = (acc1 + acc3).astype(out_ref.dtype)
            out_ref[0, s, rs, bins:] = (acc1 + acc2).astype(out_ref.dtype)
        return carry

    lax.fori_loop(0, src_ref.shape[2], body, 0)


def cross_part(entries, pos, rcv_t, buf=None):
    m, nb, piece, windows, width = entries.shape
    receivers = rcv_t.shape[2]
    qc = SOURCE // piece
    flops = 6 * nb * m * piece * receivers * windows * (width // 2)
    in_specs = [
        pl.BlockSpec((1, 1, piece, windows, width), lambda k, i, o: (i, k, 0, 0, 0)),
        pl.BlockSpec((3, windows, receivers, width // 2), lambda k, i, o: (0, 0, 0, 0)),
    ]
    args = [pos, entries, rcv_t]
    aliases = {}
    if buf is not None:
        in_specs.append(pl.BlockSpec(memory_space=pl.ANY))
        args.append(buf)
        aliases = {3: 0}
    return pl.pallas_call(
        cross_kernel,
        grid_spec=pltpu.PrefetchScalarGridSpec(
            num_scalar_prefetch=1,
            grid=(nb, m),
            in_specs=in_specs,
            out_specs=pl.BlockSpec((1, piece, receivers, width), lambda k, i, o: (k, o[i], 0, 0)),
        ),
        out_shape=jax.ShapeDtypeStruct((nb, qc * piece, receivers, width), jnp.bfloat16),
        input_output_aliases=aliases,
        cost_estimate=pl.CostEstimate(
            flops=flops,
            bytes_accessed=entries.size * 2 + rcv_t.size * 4 + nb * m * piece * receivers * width * 2,
            transcendentals=0,
        ),
    )(*args)


def plane_size(mesh):
    devs = list(mesh.devices[0])
    n = len(devs)
    best = 1
    for axis in range(3):
        first = next((i for i, d in enumerate(devs) if d.coords[axis] != devs[0].coords[axis]), None)
        if first is not None and first > best:
            best = first
    if best >= n or n % best:
        best = 1
    return best


def pairs_of(n, fn):
    out = []
    for i in range(n):
        j = fn(i)
        if j is not None:
            out.append((i, j))
    return out


def make_shards(n, qc):
    zc = n // qc
    plane_bits = [1 << b for b in reversed(range(qc.bit_length() - 1))]

    def shards(spectra, source_blocks, window_valid):
        receivers, windows, width = spectra.shape
        bins = width // 2
        me = lax.axis_index("chan")
        z = me // qc
        q = me % qc
        blocks = source_blocks.reshape(-1)
        nb = blocks.shape[0]
        zk = blocks // qc
        qk = blocks % qc
        piece = SOURCE // qc

        own = spectra.reshape(qc, piece, windows, width)
        by_off = [lax.dynamic_index_in_dim(own, q, 0, keepdims=False)]
        for d in range(1, qc):
            send = lax.dynamic_index_in_dim(own, q ^ d, 0, keepdims=False)
            by_off.append(
                lax.ppermute(send, "chan", pairs_of(n, lambda i, d=d: (i // qc) * qc + ((i % qc) ^ d)))
            )
        by_off = jnp.stack(by_off)

        here = zk == z
        sel = jnp.take(by_off, qk ^ q, axis=0)
        payload = jnp.where(here[:, None, None, None], sel, jnp.zeros_like(sel))

        mask = here[:, None, None, None]
        if zc & (zc - 1) == 0:
            mine = payload
            d = 1
            while d < zc:
                got = lax.ppermute(
                    mine, "chan", pairs_of(n, lambda i, d=d: (((i // qc) ^ d) * qc) + i % qc)
                )
                valid = (((zk ^ z) & ~(d - 1)) == 0)[:, None, None, None]
                mine = jnp.where(valid, mine, got)
                d *= 2
        else:
            up_pairs = pairs_of(n, lambda i: i + qc if i // qc < zc - 1 else None)
            down_pairs = pairs_of(n, lambda i: i - qc if i // qc > 0 else None)
            cur_up, cur_down = payload, payload
            rec_up, rec_down = payload, payload
            for r in range(zc - 1):
                rec_up = lax.ppermute(cur_up, "chan", up_pairs)
                rec_down = lax.ppermute(cur_down, "chan", down_pairs)
                if r < zc - 2:
                    cur_up = jnp.where(mask, payload, rec_up)
                    cur_down = jnp.where(mask, payload, rec_down)
            below = (z > zk)[:, None, None, None]
            mine = jnp.where(mask, payload, jnp.where(below, rec_up, rec_down))

        lag_table = build_table(bins, LAGS)
        window_mask = window_valid.astype(jnp.float32)[:, None, None]
        rcv_t = jnp.transpose(spectra, (1, 0, 2)).astype(jnp.float32) * window_mask
        rc, rd = rcv_t[..., :bins], rcv_t[..., bins:]
        rcv_t = jnp.stack([rc, rd - rc, rc + rd])

        def xor_pairs(b):
            return pairs_of(n, lambda i: (i // qc) * qc + ((i % qc) ^ b))

        if qc == 4:
            from_y = lax.ppermute(mine, "chan", xor_pairs(2))
            from_c = lax.ppermute(mine, "chan", xor_pairs(1))
            cross = cross_part(mine[None], q[None].astype(jnp.int32), rcv_t)
            cross = cross_part(from_c[None], (q ^ 1)[None].astype(jnp.int32), rcv_t, cross)
            from_yc = lax.ppermute(from_y, "chan", xor_pairs(1))
            cross = cross_part(from_y[None], (q ^ 2)[None].astype(jnp.int32), rcv_t, cross)
            cross = cross_part(from_yc[None], (q ^ 3)[None].astype(jnp.int32), rcv_t, cross)
        else:
            cross = cross_part(mine[None], q[None].astype(jnp.int32), rcv_t)
            offs = [0]
            held = [mine]
            for b in plane_bits:
                got = lax.ppermute(jnp.stack(held), "chan", pairs_of(n, lambda i, b=b: (i // qc) * qc + ((i % qc) ^ b)))
                new_offs = [o ^ b for o in offs]
                pos = q ^ jnp.array(new_offs, jnp.int32)
                cross = cross_part(got, pos, rcv_t, cross)
                offs = offs + new_offs
                held = held + [got[i] for i in range(got.shape[0])]
        traces = jnp.dot(
            cross.reshape(nb * SOURCE * receivers, width), lag_table, preferred_element_type=jnp.float32
        ).reshape(nb, SOURCE, receivers, LAGS)
        peak = jnp.max(jnp.abs(traces), axis=(2, 3))
        got = [
            lax.ppermute(peak, "chan", pairs_of(n, lambda i, d=d: (i // qc) * qc + ((i % qc) ^ d)))
            for d in range(1, qc)
        ]
        for g in got:
            peak = jnp.maximum(peak, g)
        got = [
            lax.ppermute(peak, "chan", pairs_of(n, lambda i, d=d: ((i // qc + d) % zc) * qc + i % qc))
            for d in range(1, zc)
        ]
        for g in got:
            peak = jnp.maximum(peak, g)
        normed = (traces / (peak[:, :, None, None] + 1e-06)).astype(jnp.bfloat16)
        return normed.reshape(source_blocks.shape[0], source_blocks.shape[1], SOURCE, receivers, LAGS)

    return shards


def solution(mesh):
    n = mesh.shape["chan"]
    qc = plane_size(mesh)
    placed = (P(("parts", "chan"), None, None), P("parts", None), P("parts"))
    inner = make_shards(n, qc)

    return jax.shard_map(
        inner,
        mesh=mesh,
        in_specs=placed,
        out_specs=P(None, None, None, ("parts", "chan"), None),
        check_vma=False,
    )
```
